32 devices in a mesh: blk: 4 (over x, core), rep: 8 (over z, y).
Axes of the slice: x: 2, y: 2, z: 4, core: 2. Of those that a mesh axis runs over, the one named last changes fastest.
Arguments:
- features: bfloat16 [4096, 256], P(('blk', 'rep')), may hold values from -6 to 6
- weight_one: bfloat16 [256, 256], replicated, may hold values from -0.375 to 0.375
- weight_two: bfloat16 [256, 256], replicated, may hold values from -0.375 to 0.375
- tile_values: bfloat16 [4, 8, 24, 128, 128], P('blk', 'rep'), may hold values from -0.125 to 0.125
- tile_rows: int32 [4, 8, 24], P('blk', 'rep'), may hold values from 0 to 7, as said below
- tile_cols: int32 [4, 8, 24], P('blk', 'rep'), may hold values from 0 to 31, as said below
- tile_count: int32 [4, 8], P('blk', 'rep'), may hold values from 16 to 24, as said below
Outputs:
- aggregated: bfloat16 [4096, 256], P(('blk', 'rep'))
The draws below stay inside these ranges and needn't reach their ends.
Inputs may be any that keep to these rules, and one draw needn't show every extreme that they name: `tile_rows`: block row within the holder's row group into which a tile adds; slots k >= tile_count are ignored. `tile_cols`: A tile held at rep index r has column block j * 8 + r for some j: its columns are nodes held by a device of rep index r. `tile_count`: one device holds exactly 24 live tiles.
All inputs are finite; a program needn't handle non-finite values.
Results may differ from the reference program's by a relative error of at most 0.035.
Values may be sent and summed in bfloat16 or wider, within the bound.
No kernel may reach another device: no remote copies, remote signals or barrier semaphores. Data moves between devices by JAX's collectives and lax.ppermute only.
A program may use at most 64 MiB of HBM per device.

```python
import jax
import jax.numpy as jnp
from jax import lax

B = 128
F = 256
BR_DEV = 1
CAP_ROW = 24
CAP = 24
GB = 8
BLOCKS = 32
NODES = 4096
N_BLK = 4
N_REP = 8


def draw_tile_rows(key, part):
    shape_all = (N_BLK, N_REP, CAP)
    offset = jax.random.randint(jax.random.fold_in(key, 11), (N_BLK, N_REP, 1), 0, GB, dtype=jnp.int32)
    stride = 1 + 2 * jax.random.randint(jax.random.fold_in(key, 12), (N_BLK, N_REP, 1), 0, GB, dtype=jnp.int32)
    slot_ids = lax.broadcasted_iota(jnp.int32, shape_all, 2)
    return ((offset + slot_ids * stride) % GB).astype(jnp.int32)


def draw_tile_cols(key, part):
    shape_all = (N_BLK, N_REP, CAP)
    group_pick = jax.random.randint(jax.random.fold_in(key, 21), shape_all, 0, N_BLK, dtype=jnp.int32)
    sub_pick = jax.random.randint(jax.random.fold_in(key, 22), shape_all, 0, BR_DEV, dtype=jnp.int32)
    slot_ids = lax.broadcasted_iota(jnp.int32, shape_all, 1)
    return (group_pick * N_REP + slot_ids) * BR_DEV + sub_pick


def draw_tile_count(key, part):
    base_count = CAP - CAP // 3
    level = jax.random.randint(jax.random.fold_in(key, 31), (N_BLK, N_REP), 0, CAP, dtype=jnp.int32)
    counted = base_count + level * (CAP - base_count) // CAP
    total_devs = N_BLK * N_REP
    chosen = jax.random.randint(jax.random.fold_in(key, 32), (), 0, total_devs, dtype=jnp.int32)
    lowest = (chosen + 1) % total_devs
    flat_ids = lax.broadcasted_iota(jnp.int32, (N_BLK, N_REP), 0) * N_REP + lax.broadcasted_iota(jnp.int32, (N_BLK, N_REP), 1)
    counted = jnp.where(flat_ids == lowest, base_count, counted)
    return jnp.where(flat_ids == chosen, CAP, counted).astype(jnp.int32)


def levels(key, shape, split, low, top_value):
    factor_of, own = 1.0, jax.random.fold_in(key, 6)
    for position, parts in split:
        steps = jnp.exp(jax.random.uniform(jax.random.fold_in(own, position), (parts,), jnp.float32, low / len(split), top_value / len(split)))
        factor_of = factor_of * jnp.repeat(steps, shape[position] // parts).reshape([-1 if axis == position else 1 for axis in range(len(shape))])
    return factor_of


def bell_draw(stream_key, extent, deviation, most, split=(), kind=jnp.bfloat16):
    factor_of = levels(stream_key, extent, split, -0.22, 0.18) if split else 1.0
    entries = jax.random.normal(stream_key, extent, jnp.float32) * deviation * factor_of
    return jnp.minimum(jnp.maximum(entries, -most), most).astype(kind)


def setup_inputs(seed: int = 0) -> dict:
    key_list = jax.random.split(jax.random.key(seed), 8)
    return {
        "features": bell_draw(key_list[0], (NODES, F), 1.0, 6.0, ((0, 32),)),
        "weight_one": bell_draw(key_list[1], (F, F), F ** -0.5, 0.375),
        "weight_two": bell_draw(key_list[2], (F, F), F ** -0.5, 0.375),
        "tile_values": bell_draw(key_list[3], (N_BLK, N_REP, CAP, B, B), (CAP_ROW * B * 2 // 3) ** -0.5, 0.125, ((0, 4), (1, 8))),
        "tile_rows": draw_tile_rows(jax.random.fold_in(key_list[7], 71), 0),
        "tile_cols": draw_tile_cols(jax.random.fold_in(key_list[7], 71), 0),
        "tile_count": draw_tile_count(jax.random.fold_in(key_list[7], 71), 0),
    }


def aggregate(panel_rows, tile_values, tile_rows, tile_cols, tile_count):
    node_blocks = panel_rows.reshape(BLOCKS, B, F)
    slot_ids = jnp.arange(CAP).astype(jnp.int32)
    group_ids = jnp.arange(GB).astype(jnp.int32)

    def one_device(unused, inputs):
        tile_vals, row_ids, col_ids, live_count = inputs
        source = node_blocks[col_ids.astype(jnp.int32)]
        products = jnp.einsum("kab,kbf->kaf", tile_vals.astype(jnp.float32), source.astype(jnp.float32), precision=lax.Precision.HIGHEST)
        placing = ((row_ids[:, None] == group_ids[None, :]) & (slot_ids < live_count)[:, None]).astype(jnp.float32)
        partial_value = jnp.einsum("kg,kaf->gaf", placing, products, precision=lax.Precision.HIGHEST)
        return unused, partial_value.astype(jnp.bfloat16)

    def one_group(unused, inputs):
        unused_two, slot_parts = lax.scan(one_device, unused, inputs)
        return unused, jnp.sum(slot_parts.astype(jnp.float32), axis=0)

    unused_end, group_sums = lax.scan(one_group, jnp.float32(0.0), (tile_values, tile_rows, tile_cols, tile_count))
    return group_sums.reshape(NODES, F)


def reference(features, weight_one, weight_two, tile_values, tile_rows, tile_cols, tile_count):
    panel_one = jnp.dot(features, weight_one, preferred_element_type=jnp.float32).astype(jnp.bfloat16)
    sum_one = aggregate(panel_one, tile_values, tile_rows, tile_cols, tile_count)
    hidden = jnp.maximum(sum_one, 0.0).astype(jnp.bfloat16)
    panel_two = jnp.dot(hidden, weight_two, preferred_element_type=jnp.float32).astype(jnp.bfloat16)
    sum_two = aggregate(panel_two, tile_values, tile_rows, tile_cols, tile_count)
    return sum_two.astype(jnp.bfloat16)
```

```python
import functools

import jax
import jax.numpy as jnp
from jax import lax
from jax.experimental import pallas as pl
from jax.experimental.pallas import tpu as pltpu
from jax.sharding import PartitionSpec as P


def _agg_kernel(rows_ref, blks_ref, cnt_ref, panel_ref, tiles_ref, out_ref, acc_ref):
    acc_ref[...] = jnp.zeros_like(acc_ref)
    live = cnt_ref[0]
    n_rows = acc_ref.shape[0]
    n_src = panel_ref.shape[0]

    def step(k, carry):
        @pl.when(k < live)
        def _():
            row = jnp.clip(rows_ref[k], 0, n_rows - 1)
            src = jnp.clip(blks_ref[k], 0, n_src - 1)
            acc_ref[row] += jnp.dot(tiles_ref[k], panel_ref[src], preferred_element_type=jnp.float32)

        return carry

    lax.fori_loop(0, tiles_ref.shape[0], step, 0)
    out_ref[...] = acc_ref[...].astype(out_ref.dtype)


def aggregate(panel_blocks, tile_vals, tile_row, src_block, live_count, n_rows):
    slots, blk, _ = tile_vals.shape
    feat = panel_blocks.shape[-1]
    smem = pl.BlockSpec(memory_space=pltpu.SMEM)
    vmem = pl.BlockSpec(memory_space=pltpu.VMEM)
    flops = 2 * slots * blk * blk * feat
    nbytes = 2 * (panel_blocks.size + tile_vals.size + n_rows * blk * feat)
    return pl.pallas_call(
        _agg_kernel,
        out_shape=jax.ShapeDtypeStruct((n_rows, blk, feat), jnp.bfloat16),
        in_specs=[smem, smem, smem, vmem, vmem],
        out_specs=vmem,
        scratch_shapes=[pltpu.VMEM((n_rows, blk, feat), jnp.float32)],
        cost_estimate=pl.CostEstimate(flops=flops, bytes_accessed=nbytes, transcendentals=0),
    )(tile_row, src_block, live_count.reshape(1), panel_blocks, tile_vals)


def gather_blk(panel, mode):
    n = lax.axis_size("blk")
    if mode == "ag":
        return lax.all_gather(panel, "blk", axis=0, tiled=False)
    me = lax.axis_index("blk")
    pieces = [panel]
    for s in range(1, n):
        perm = [(src, (src + s) % n) for src in range(n)]
        pieces.append(lax.ppermute(panel, "blk", perm))
    stacked = jnp.stack(pieces)
    order = (me - jnp.arange(n)) % n
    inv = jnp.argsort(order)
    return stacked[inv]


def exchange_rep(partial, mode):
    n = lax.axis_size("rep")
    if mode == "rs":
        flat = partial.reshape(-1, partial.shape[-1])
        return lax.psum_scatter(flat, "rep", scatter_dimension=0, tiled=True).astype(jnp.float32)
    if mode == "a2a":
        got = lax.all_to_all(partial, "rep", 0, 0, tiled=True)
        return jnp.sum(got.astype(jnp.float32), axis=0)
    me = lax.axis_index("rep")
    total = lax.dynamic_index_in_dim(partial, me, 0, keepdims=False).astype(jnp.float32)
    for s in range(1, n):
        perm = [(src, (src + s) % n) for src in range(n)]
        piece = lax.dynamic_index_in_dim(partial, (me + s) % n, 0, keepdims=False)
        total = total + lax.ppermute(piece, "rep", perm).astype(jnp.float32)
    return total


def make_body(gmode, xmode):
    def body(features, weight_one, weight_two, tile_values, tile_rows, tile_cols, tile_count):
        tile_vals = tile_values[0, 0]
        tile_row = tile_rows[0, 0]
        tile_col = tile_cols[0, 0]
        live_count = tile_count[0, 0]
        replicas = lax.axis_size("rep")
        src_block = tile_col // replicas
        hidden = features
        for layer_id in range(2):
            weight = weight_one if layer_id == 0 else weight_two
            panel = jnp.dot(hidden, weight, preferred_element_type=jnp.float32).astype(jnp.bfloat16)
            blocks = gather_blk(panel, gmode)
            partial = aggregate(blocks, tile_vals, tile_row, src_block, live_count, replicas)
            summed = exchange_rep(partial, xmode)
            if layer_id == 0:
                hidden = jnp.maximum(summed, 0.0).astype(jnp.bfloat16)
            else:
                return summed.astype(jnp.bfloat16)

    return body


def solution(mesh, gmode="ag", xmode="pp"):
    in_specs = (
        P(("blk", "rep"), None),
        P(),
        P(),
        P("blk", "rep", None, None, None),
        P("blk", "rep", None),
        P("blk", "rep", None),
        P("blk", "rep"),
    )
    out_specs = P(("blk", "rep"), None)
    return jax.shard_map(make_body(gmode, xmode), mesh=mesh, in_specs=in_specs, out_specs=out_specs, check_vma=False)
```

```python
import jax
import jax.numpy as jnp
from jax import lax
from jax.experimental import pallas as pl
from jax.experimental.pallas import tpu as pltpu
from jax.sharding import PartitionSpec as P


def _agg_kernel(rows_ref, blks_ref, panel_ref, tiles_ref, *rest):
    out_refs, acc_ref = rest[:-1], rest[-1]
    acc_ref[...] = jnp.zeros_like(acc_ref)
    for k in range(tiles_ref.shape[0]):
        acc_ref[rows_ref[k]] += jnp.dot(
            tiles_ref[k], panel_ref[blks_ref[k]], preferred_element_type=jnp.float32
        )
    for s, out_ref in enumerate(out_refs):
        out_ref[...] = acc_ref[s].astype(out_ref.dtype)


def aggregate(panel_blocks, tile_vals, send_row, src_block, n_rows):
    slots, blk, _ = tile_vals.shape
    feat = panel_blocks.shape[-1]
    smem = pl.BlockSpec(memory_space=pltpu.SMEM)
    vmem = pl.BlockSpec(memory_space=pltpu.VMEM)
    flops = 2 * slots * blk * blk * feat
    nbytes = 2 * (panel_blocks.size + tile_vals.size + n_rows * blk * feat)
    return pl.pallas_call(
        _agg_kernel,
        out_shape=[jax.ShapeDtypeStruct((blk, feat), jnp.bfloat16) for _ in range(n_rows)],
        in_specs=[smem, smem, vmem, vmem],
        out_specs=[vmem] * n_rows,
        scratch_shapes=[pltpu.VMEM((n_rows + 1, blk, feat), jnp.float32)],
        cost_estimate=pl.CostEstimate(flops=flops, bytes_accessed=nbytes, transcendentals=0),
    )(send_row, src_block, panel_blocks, tile_vals)


def exchange_rep(partial):
    n = lax.axis_size("rep")
    total = partial[0].astype(jnp.float32)
    for s in range(1, n):
        perm = [(src, (src + s) % n) for src in range(n)]
        total = total + lax.ppermute(partial[s], "rep", perm).astype(jnp.float32)
    return total


def make_body():
    def body(features, weight_one, weight_two, tile_values, tile_rows, tile_cols, tile_count):
        tile_vals = tile_values[0, 0]
        tile_row = tile_rows[0, 0]
        tile_col = tile_cols[0, 0]
        live_count = tile_count[0, 0]
        replicas = lax.axis_size("rep")
        n_src = lax.axis_size("blk")
        me = lax.axis_index("rep")
        slot_ids = lax.iota(jnp.int32, tile_row.shape[0])
        send_row = jnp.where(
            slot_ids < live_count, (jnp.clip(tile_row, 0, replicas - 1) - me) % replicas, replicas
        )
        src_block = jnp.clip(tile_col // replicas, 0, n_src - 1)
        hidden = features
        for layer_id in range(2):
            weight = weight_one if layer_id == 0 else weight_two
            panel = jnp.dot(hidden, weight, preferred_element_type=jnp.float32).astype(jnp.bfloat16)
            blocks = lax.all_gather(panel, "blk", axis=0, tiled=False)
            partial = aggregate(blocks, tile_vals, send_row, src_block, replicas)
            summed = exchange_rep(partial)
            if layer_id == 0:
                hidden = jnp.maximum(summed, 0.0).astype(jnp.bfloat16)
            else:
                return summed.astype(jnp.bfloat16)

    return body


def solution(mesh):
    in_specs = (
        P(("blk", "rep"), None),
        P(),
        P(),
        P("blk", "rep", None, None, None),
        P("blk", "rep", None),
        P("blk", "rep", None),
        P("blk", "rep"),
    )
    out_specs = P(("blk", "rep"), None)
    return jax.shard_map(make_body(), mesh=mesh, in_specs=in_specs, out_specs=out_specs, check_vma=False)
```

```python
import jax
import jax.numpy as jnp
from jax import lax
from jax.experimental import pallas as pl
from jax.experimental.pallas import tpu as pltpu
from jax.sharding import PartitionSpec as P


def _agg_kernel(rows_ref, blks_ref, panel_ref, tiles_ref, *rest):
    out_refs, acc_ref = rest[:-1], rest[-1]
    acc_ref[...] = jnp.zeros_like(acc_ref)
    for k in range(tiles_ref.shape[0]):
        acc_ref[rows_ref[k]] += jnp.dot(
            tiles_ref[k], panel_ref[blks_ref[k]], preferred_element_type=jnp.float32
        )
    for s, out_ref in enumerate(out_refs):
        out_ref[...] = acc_ref[s].astype(out_ref.dtype)


def aggregate(panel_blocks, tile_vals, send_row, src_block, n_rows):
    slots, blk, _ = tile_vals.shape
    feat = panel_blocks.shape[-1]
    smem = pl.BlockSpec(memory_space=pltpu.SMEM)
    vmem = pl.BlockSpec(memory_space=pltpu.VMEM)
    flops = 2 * slots * blk * blk * feat
    nbytes = 2 * (panel_blocks.size + tile_vals.size + n_rows * blk * feat)
    return pl.pallas_call(
        _agg_kernel,
        out_shape=[jax.ShapeDtypeStruct((blk, feat), jnp.bfloat16) for _ in range(n_rows)],
        in_specs=[smem, smem, vmem, vmem],
        out_specs=[vmem] * n_rows,
        scratch_shapes=[pltpu.VMEM((n_rows + 1, blk, feat), jnp.float32)],
        cost_estimate=pl.CostEstimate(flops=flops, bytes_accessed=nbytes, transcendentals=0),
    )(send_row, src_block, panel_blocks, tile_vals)


def exchange_rep(partial):
    n = lax.axis_size("rep")
    outer = n // 2
    pair = [(src, src ^ 1) for src in range(n)]
    total = None
    for t in range(outer):
        got = lax.ppermute(partial[t * 2 + 1], "rep", pair)
        both = partial[t * 2].astype(jnp.float32) + got.astype(jnp.float32)
        if t == 0:
            total = both
            continue
        perm = [(src, ((src // 2 + t) % outer) * 2 + src % 2) for src in range(n)]
        total = total + lax.ppermute(both.astype(jnp.bfloat16), "rep", perm).astype(jnp.float32)
    return total


def make_body():
    def body(features, weight_one, weight_two, tile_values, tile_rows, tile_cols, tile_count):
        tile_vals = tile_values[0, 0]
        tile_row = tile_rows[0, 0]
        tile_col = tile_cols[0, 0]
        live_count = tile_count[0, 0]
        replicas = lax.axis_size("rep")
        n_src = lax.axis_size("blk")
        me = lax.axis_index("rep")
        slot_ids = lax.iota(jnp.int32, tile_row.shape[0])
        row = jnp.clip(tile_row, 0, replicas - 1)
        outer = replicas // 2
        send_pos = ((row // 2 - me // 2) % outer) * 2 + ((row % 2) ^ (me % 2))
        send_row = jnp.where(slot_ids < live_count, send_pos, replicas)
        src_block = jnp.clip(tile_col // replicas, 0, n_src - 1)
        hidden = features
        for layer_id in range(2):
            weight = weight_one if layer_id == 0 else weight_two
            panel = jnp.dot(hidden, weight, preferred_element_type=jnp.float32).astype(jnp.bfloat16)
            blocks = lax.all_gather(panel, "blk", axis=0, tiled=False)
            partial = aggregate(blocks, tile_vals, send_row, src_block, replicas)
            summed = exchange_rep(partial)
            if layer_id == 0:
                hidden = jnp.maximum(summed, 0.0).astype(jnp.bfloat16)
            else:
                return summed.astype(jnp.bfloat16)

    return body


def solution(mesh):
    in_specs = (
        P(("blk", "rep"), None),
        P(),
        P(),
        P("blk", "rep", None, None, None),
        P("blk", "rep", None),
        P("blk", "rep", None),
        P("blk", "rep"),
    )
    out_specs = P(("blk", "rep"), None)
    return jax.shard_map(make_body(), mesh=mesh, in_specs=in_specs, out_specs=out_specs, check_vma=False)
```

```python
import jax
import jax.numpy as jnp
from jax import lax
from jax.experimental import pallas as pl
from jax.experimental.pallas import tpu as pltpu
from jax.sharding import PartitionSpec as P


def _agg_kernel(rows_ref, cols_ref, cnt_ref, panel_ref, tiles_ref, *rest):
    out_refs, acc_ref = rest[:-1], rest[-1]
    n_rows = len(out_refs)
    outer = n_rows // 2
    n_src = panel_ref.shape[0]
    me = lax.axis_index("rep")
    live = cnt_ref[0]
    acc_ref[...] = jnp.zeros_like(acc_ref)
    for k in range(tiles_ref.shape[0]):
        row = jnp.clip(rows_ref[k], 0, n_rows - 1)
        step = (row // 2 - me // 2 + outer) % outer
        pos = step * 2 + (row % 2 + me % 2) % 2
        dest = jnp.where(k < live, pos, n_rows)
        src = jnp.clip(cols_ref[k] // n_rows, 0, n_src - 1)
        acc_ref[dest] += jnp.dot(tiles_ref[k], panel_ref[src], preferred_element_type=jnp.float32)
    for s, out_ref in enumerate(out_refs):
        out_ref[...] = acc_ref[s].astype(out_ref.dtype)


def aggregate(panel_blocks, tile_vals, tile_row, tile_col, live_count, n_rows):
    slots, blk, _ = tile_vals.shape
    feat = panel_blocks.shape[-1]
    smem = pl.BlockSpec(memory_space=pltpu.SMEM)
    vmem = pl.BlockSpec(memory_space=pltpu.VMEM)
    flops = 2 * slots * blk * blk * feat
    nbytes = 2 * (panel_blocks.size + tile_vals.size + n_rows * blk * feat)
    return pl.pallas_call(
        _agg_kernel,
        out_shape=[jax.ShapeDtypeStruct((blk, feat), jnp.bfloat16) for _ in range(n_rows)],
        in_specs=[smem, smem, smem, vmem, vmem],
        out_specs=[vmem] * n_rows,
        scratch_shapes=[pltpu.VMEM((n_rows + 1, blk, feat), jnp.float32)],
        cost_estimate=pl.CostEstimate(flops=flops, bytes_accessed=nbytes, transcendentals=0),
    )(tile_row, tile_col, live_count.reshape(1), panel_blocks, tile_vals)


def exchange_rep(partial):
    n = lax.axis_size("rep")
    outer = n // 2
    pair = [(src, src ^ 1) for src in range(n)]
    total = None
    for t in range(outer):
        got = lax.ppermute(partial[t * 2 + 1], "rep", pair)
        both = partial[t * 2].astype(jnp.float32) + got.astype(jnp.float32)
        if t == 0:
            total = both
            continue
        perm = [(src, ((src // 2 + t) % outer) * 2 + src % 2) for src in range(n)]
        total = total + lax.ppermute(both.astype(jnp.bfloat16), "rep", perm).astype(jnp.float32)
    return total


def make_body():
    def body(features, weight_one, weight_two, tile_values, tile_rows, tile_cols, tile_count):
        tile_vals = tile_values[0, 0]
        tile_row = tile_rows[0, 0]
        tile_col = tile_cols[0, 0]
        live_count = tile_count[0, 0]
        replicas = lax.axis_size("rep")
        hidden = features
        for layer_id in range(2):
            weight = weight_one if layer_id == 0 else weight_two
            panel = jnp.dot(hidden, weight, preferred_element_type=jnp.float32).astype(jnp.bfloat16)
            blocks = lax.all_gather(panel, "blk", axis=0, tiled=False)
            partial = aggregate(blocks, tile_vals, tile_row, tile_col, live_count, replicas)
            summed = exchange_rep(partial)
            if layer_id == 0:
                hidden = jnp.maximum(summed, 0.0).astype(jnp.bfloat16)
            else:
                return summed.astype(jnp.bfloat16)

    return body


def solution(mesh):
    in_specs = (
        P(("blk", "rep"), None),
        P(),
        P(),
        P("blk", "rep", None, None, None),
        P("blk", "rep", None),
        P("blk", "rep", None),
        P("blk", "rep"),
    )
    out_specs = P(("blk", "rep"), None)
    return jax.shard_map(make_body(), mesh=mesh, in_specs=in_specs, out_specs=out_specs, check_vma=False)
```

```python
import jax
import jax.numpy as jnp
from jax import lax
from jax.experimental import pallas as pl
from jax.experimental.pallas import tpu as pltpu
from jax.sharding import PartitionSpec as P


def _agg_kernel(rows_ref, cols_ref, cnt_ref, panel_ref, tiles_ref, *rest):
    out_refs, acc_ref = rest[:-1], rest[-1]
    n_rows = len(out_refs)
    outer = n_rows // 2
    n_src = panel_ref.shape[0]
    me = lax.axis_index("rep")
    live = cnt_ref[0]
    acc_ref[...] = jnp.zeros_like(acc_ref)
    for k in range(tiles_ref.shape[0]):
        row = jnp.clip(rows_ref[k], 0, n_rows - 1)
        step = (row // 2 - me // 2 + outer) % outer
        pos = step * 2 + (row % 2 + me % 2) % 2
        dest = jnp.where(k < live, pos, n_rows)
        src = jnp.clip(cols_ref[k] // n_rows, 0, n_src - 1)
        acc_ref[dest] += jnp.dot(tiles_ref[k], panel_ref[src], preferred_element_type=jnp.float32)
    for s, out_ref in enumerate(out_refs):
        out_ref[...] = acc_ref[s].astype(out_ref.dtype)


def aggregate(panel_blocks, tile_vals, tile_row, tile_col, live_count, n_rows):
    slots, blk, _ = tile_vals.shape
    feat = panel_blocks.shape[-1]
    smem = pl.BlockSpec(memory_space=pltpu.SMEM)
    vmem = pl.BlockSpec(memory_space=pltpu.VMEM)
    flops = 2 * slots * blk * blk * feat
    nbytes = 2 * (panel_blocks.size + tile_vals.size + n_rows * blk * feat)
    return pl.pallas_call(
        _agg_kernel,
        out_shape=[jax.ShapeDtypeStruct((blk, feat), jnp.bfloat16) for _ in range(n_rows)],
        in_specs=[smem, smem, smem, vmem, vmem],
        out_specs=[vmem] * n_rows,
        scratch_shapes=[pltpu.VMEM((n_rows + 1, blk, feat), jnp.float32)],
        cost_estimate=pl.CostEstimate(flops=flops, bytes_accessed=nbytes, transcendentals=0),
    )(tile_row, tile_col, live_count.reshape(1), panel_blocks, tile_vals)


def exchange_rep(partial):
    n = lax.axis_size("rep")
    outer = n // 2
    pair = [(src, src ^ 1) for src in range(n)]
    order = list(range(1, outer)) + [0]
    got = {t: lax.ppermute(partial[t * 2 + 1], "rep", pair) for t in order}
    total = None
    for t in order:
        both = partial[t * 2].astype(jnp.float32) + got[t].astype(jnp.float32)
        if t == 0:
            piece = both
        else:
            perm = [(src, ((src // 2 + t) % outer) * 2 + src % 2) for src in range(n)]
            piece = lax.ppermute(both.astype(jnp.bfloat16), "rep", perm).astype(jnp.float32)
        total = piece if total is None else total + piece
    return total


def make_body():
    def body(features, weight_one, weight_two, tile_values, tile_rows, tile_cols, tile_count):
        tile_vals = tile_values[0, 0]
        tile_row = tile_rows[0, 0]
        tile_col = tile_cols[0, 0]
        live_count = tile_count[0, 0]
        replicas = lax.axis_size("rep")
        hidden = features
        for layer_id in range(2):
            weight = weight_one if layer_id == 0 else weight_two
            panel = jnp.dot(hidden, weight, preferred_element_type=jnp.float32).astype(jnp.bfloat16)
            blocks = lax.all_gather(panel, "blk", axis=0, tiled=False)
            partial = aggregate(blocks, tile_vals, tile_row, tile_col, live_count, replicas)
            summed = exchange_rep(partial)
            if layer_id == 0:
                hidden = jnp.maximum(summed, 0.0).astype(jnp.bfloat16)
            else:
                return summed.astype(jnp.bfloat16)

    return body


def solution(mesh):
    in_specs = (
        P(("blk", "rep"), None),
        P(),
        P(),
        P("blk", "rep", None, None, None),
        P("blk", "rep", None),
        P("blk", "rep", None),
        P("blk", "rep"),
    )
    out_specs = P(("blk", "rep"), None)
    return jax.shard_map(make_body(), mesh=mesh, in_specs=in_specs, out_specs=out_specs, check_vma=False)
```

```python
import jax
import jax.numpy as jnp
from jax import lax
from jax.experimental import pallas as pl
from jax.experimental.pallas import tpu as pltpu
from jax.sharding import PartitionSpec as P


def _agg_kernel(rows_ref, cols_ref, cnt_ref, panel_ref, tiles_ref, *rest):
    out_refs, acc_ref = rest[:-1], rest[-1]
    n_rows = len(out_refs)
    outer = n_rows // 2
    n_src = panel_ref.shape[0]
    me = lax.axis_index("rep")
    live = cnt_ref[0]
    acc_ref[...] = jnp.zeros_like(acc_ref)
    for k in range(tiles_ref.shape[0]):
        row = jnp.clip(rows_ref[k], 0, n_rows - 1)
        step = (row // 2 - me // 2 + outer) % outer
        pos = step * 2 + (row % 2 + me % 2) % 2
        dest = jnp.where(k < live, pos, n_rows)
        src = jnp.clip(cols_ref[k] // n_rows, 0, n_src - 1)
        acc_ref[dest] += jnp.dot(tiles_ref[k], panel_ref[src], preferred_element_type=jnp.float32)
    for s, out_ref in enumerate(out_refs):
        out_ref[...] = acc_ref[s].astype(out_ref.dtype)


def aggregate(panel_blocks, tile_vals, tile_row, tile_col, live_count, n_rows):
    slots, blk, _ = tile_vals.shape
    feat = panel_blocks.shape[-1]
    smem = pl.BlockSpec(memory_space=pltpu.SMEM)
    vmem = pl.BlockSpec(memory_space=pltpu.VMEM)
    flops = 2 * slots * blk * blk * feat
    nbytes = 2 * (panel_blocks.size + tile_vals.size + n_rows * blk * feat)
    return pl.pallas_call(
        _agg_kernel,
        out_shape=[pltpu.VMEM((blk, feat), jnp.bfloat16) for _ in range(n_rows)],
        in_specs=[smem, smem, smem, vmem, vmem],
        out_specs=[vmem] * n_rows,
        scratch_shapes=[pltpu.VMEM((n_rows + 1, blk, feat), jnp.float32)],
        cost_estimate=pl.CostEstimate(flops=flops, bytes_accessed=nbytes, transcendentals=0),
    )(tile_row, tile_col, live_count.reshape(1), panel_blocks, tile_vals)


def exchange_rep(partial):
    n = lax.axis_size("rep")
    outer = n // 2
    pair = [(src, src ^ 1) for src in range(n)]
    order = list(range(1, outer)) + [0]
    got = {t: lax.ppermute(partial[t * 2 + 1], "rep", pair) for t in order}
    total = None
    for t in order:
        both = partial[t * 2].astype(jnp.float32) + got[t].astype(jnp.float32)
        if t == 0:
            piece = both
        else:
            perm = [(src, ((src // 2 + t) % outer) * 2 + src % 2) for src in range(n)]
            piece = lax.ppermute(both.astype(jnp.bfloat16), "rep", perm).astype(jnp.float32)
        total = piece if total is None else total + piece
    return total


def make_body():
    def body(features, weight_one, weight_two, tile_values, tile_rows, tile_cols, tile_count):
        tile_vals = tile_values[0, 0]
        tile_row = tile_rows[0, 0]
        tile_col = tile_cols[0, 0]
        live_count = tile_count[0, 0]
        replicas = lax.axis_size("rep")
        hidden = features
        for layer_id in range(2):
            weight = weight_one if layer_id == 0 else weight_two
            panel = jnp.dot(hidden, weight, preferred_element_type=jnp.float32).astype(jnp.bfloat16)
            blocks = lax.all_gather(panel, "blk", axis=0, tiled=False)
            partial = aggregate(blocks, tile_vals, tile_row, tile_col, live_count, replicas)
            summed = exchange_rep(partial)
            if layer_id == 0:
                hidden = jnp.maximum(summed, 0.0).astype(jnp.bfloat16)
            else:
                return summed.astype(jnp.bfloat16)

    return body


def solution(mesh):
    in_specs = (
        P(("blk", "rep"), None),
        P(),
        P(),
        P("blk", "rep", None, None, None),
        P("blk", "rep", None),
        P("blk", "rep", None),
        P("blk", "rep"),
    )
    out_specs = P(("blk", "rep"), None)
    return jax.shard_map(make_body(), mesh=mesh, in_specs=in_specs, out_specs=out_specs, check_vma=False)
```

```python
import jax
import jax.numpy as jnp
from jax import lax
from jax.experimental import pallas as pl
from jax.experimental.pallas import tpu as pltpu
from jax.sharding import PartitionSpec as P


def _agg_kernel(rows_ref, cols_ref, cnt_ref, panel_ref, tiles_ref, *rest):
    out_refs, acc_ref = rest[:-1], rest[-1]
    n_rows = len(out_refs)
    outer = n_rows // 2
    n_src = panel_ref.shape[0]
    me = lax.axis_index("rep")
    live = cnt_ref[0]
    acc_ref[...] = jnp.zeros_like(acc_ref)
    for k in range(tiles_ref.shape[0]):
        row = jnp.clip(rows_ref[k], 0, n_rows - 1)
        step = (row // 2 - me // 2 + outer) % outer
        pos = step * 2 + (row % 2 + me % 2) % 2
        dest = jnp.where(k < live, pos, n_rows)
        src = jnp.clip(cols_ref[k] // n_rows, 0, n_src - 1)
        acc_ref[dest] += jnp.dot(tiles_ref[k], panel_ref[src], preferred_element_type=jnp.float32)
    for s, out_ref in enumerate(out_refs):
        out_ref[...] = acc_ref[s].astype(out_ref.dtype)


def aggregate(panel_blocks, tile_vals, tile_row, tile_col, live_count, n_rows):
    slots, blk, _ = tile_vals.shape
    feat = panel_blocks.shape[-1]
    smem = pl.BlockSpec(memory_space=pltpu.SMEM)
    vmem = pl.BlockSpec(memory_space=pltpu.VMEM)
    flops = 2 * slots * blk * blk * feat
    nbytes = 2 * (panel_blocks.size + tile_vals.size + n_rows * blk * feat)
    return pl.pallas_call(
        _agg_kernel,
        out_shape=[pltpu.VMEM((blk, feat), jnp.bfloat16) for _ in range(n_rows)],
        in_specs=[smem, smem, smem, vmem, vmem],
        out_specs=[vmem] * n_rows,
        scratch_shapes=[pltpu.VMEM((n_rows + 1, blk, feat), jnp.float32)],
        cost_estimate=pl.CostEstimate(flops=flops, bytes_accessed=nbytes, transcendentals=0),
    )(tile_row, tile_col, live_count.reshape(1), *on_chip(panel_blocks, tile_vals, n_rows))


def on_chip(panel_blocks, tile_vals, n_rows):
    blk, feat = panel_blocks.shape[1:]
    footprint = 2 * (panel_blocks.size + tile_vals.size) + (2 + 4) * n_rows * blk * feat
    if footprint > 4 * 2**20:
        return panel_blocks, tile_vals
    vmem = pltpu.MemorySpace.VMEM
    return (
        pltpu.with_memory_space_constraint(panel_blocks, vmem),
        pltpu.with_memory_space_constraint(tile_vals, vmem),
    )


def exchange_rep(partial):
    n = lax.axis_size("rep")
    outer = n // 2
    pair = [(src, src ^ 1) for src in range(n)]
    order = list(range(1, outer)) + [0]
    got = {t: lax.ppermute(partial[t * 2 + 1], "rep", pair) for t in order}
    total = None
    for t in order:
        both = partial[t * 2].astype(jnp.float32) + got[t].astype(jnp.float32)
        if t == 0:
            piece = both
        else:
            perm = [(src, ((src // 2 + t) % outer) * 2 + src % 2) for src in range(n)]
            piece = lax.ppermute(both.astype(jnp.bfloat16), "rep", perm).astype(jnp.float32)
        total = piece if total is None else total + piece
    return total


def make_body():
    def body(features, weight_one, weight_two, tile_values, tile_rows, tile_cols, tile_count):
        tile_vals = tile_values[0, 0]
        tile_row = tile_rows[0, 0]
        tile_col = tile_cols[0, 0]
        live_count = tile_count[0, 0]
        replicas = lax.axis_size("rep")
        hidden = features
        for layer_id in range(2):
            weight = weight_one if layer_id == 0 else weight_two
            panel = jnp.dot(hidden, weight, preferred_element_type=jnp.float32).astype(jnp.bfloat16)
            blocks = lax.all_gather(panel, "blk", axis=0, tiled=False)
            partial = aggregate(blocks, tile_vals, tile_row, tile_col, live_count, replicas)
            summed = exchange_rep(partial)
            if layer_id == 0:
                hidden = jnp.maximum(summed, 0.0).astype(jnp.bfloat16)
            else:
                return summed.astype(jnp.bfloat16)

    return body


def solution(mesh):
    in_specs = (
        P(("blk", "rep"), None),
        P(),
        P(),
        P("blk", "rep", None, None, None),
        P("blk", "rep", None),
        P("blk", "rep", None),
        P("blk", "rep"),
    )
    out_specs = P(("blk", "rep"), None)
    return jax.shard_map(make_body(), mesh=mesh, in_specs=in_specs, out_specs=out_specs, check_vma=False)
```

```python
import functools

import jax
import jax.numpy as jnp
from jax import lax
from jax.experimental import pallas as pl
from jax.experimental.pallas import tpu as pltpu
from jax.sharding import PartitionSpec as P


def _agg_kernel(xor_order, rows_ref, cols_ref, cnt_ref, panel_ref, tiles_ref, *rest):
    out_refs, acc_ref = rest[:-1], rest[-1]
    n_rows = len(out_refs)
    outer = n_rows // 2
    n_src = panel_ref.shape[0]
    me = lax.axis_index("rep")
    live = cnt_ref[0]
    acc_ref[...] = jnp.zeros_like(acc_ref)
    for k in range(tiles_ref.shape[0]):
        row = jnp.clip(rows_ref[k], 0, n_rows - 1)
        step = (row // 2 - me // 2 + outer) % outer
        pos = step * 2 + (row % 2 + me % 2) % 2
        dest = jnp.where(k < live, pos, n_rows)
        src = jnp.clip(cols_ref[k] // n_rows, 0, n_src - 1)
        if xor_order:
            src = src ^ lax.axis_index("blk")
        acc_ref[dest] += jnp.dot(tiles_ref[k], panel_ref[src], preferred_element_type=jnp.float32)
    for s, out_ref in enumerate(out_refs):
        out_ref[...] = acc_ref[s].astype(out_ref.dtype)


def aggregate(panel_blocks, tile_vals, tile_row, tile_col, live_count, n_rows, xor_order):
    slots, blk, _ = tile_vals.shape
    feat = panel_blocks.shape[-1]
    smem = pl.BlockSpec(memory_space=pltpu.SMEM)
    vmem = pl.BlockSpec(memory_space=pltpu.VMEM)
    flops = 2 * slots * blk * blk * feat
    nbytes = 2 * (panel_blocks.size + tile_vals.size + n_rows * blk * feat)
    return pl.pallas_call(
        functools.partial(_agg_kernel, xor_order),
        out_shape=[pltpu.VMEM((blk, feat), jnp.bfloat16) for _ in range(n_rows)],
        in_specs=[smem, smem, smem, vmem, vmem],
        out_specs=[vmem] * n_rows,
        scratch_shapes=[pltpu.VMEM((n_rows + 1, blk, feat), jnp.float32)],
        cost_estimate=pl.CostEstimate(flops=flops, bytes_accessed=nbytes, transcendentals=0),
    )(tile_row, tile_col, live_count.reshape(1), *on_chip(panel_blocks, tile_vals, n_rows))


def on_chip(panel_blocks, tile_vals, n_rows):
    blk, feat = panel_blocks.shape[1:]
    footprint = 2 * (panel_blocks.size + tile_vals.size) + (2 + 4) * n_rows * blk * feat
    if footprint > 4 * 2**20:
        return panel_blocks, tile_vals
    vmem = pltpu.MemorySpace.VMEM
    return (
        pltpu.with_memory_space_constraint(panel_blocks, vmem),
        pltpu.with_memory_space_constraint(tile_vals, vmem),
    )


def exchange_rep(partial):
    n = lax.axis_size("rep")
    outer = n // 2
    pair = [(src, src ^ 1) for src in range(n)]
    order = list(range(1, outer)) + [0]
    got = {t: lax.ppermute(partial[t * 2 + 1], "rep", pair) for t in order}
    total = None
    for t in order:
        both = partial[t * 2].astype(jnp.float32) + got[t].astype(jnp.float32)
        if t == 0:
            piece = both
        else:
            perm = [(src, ((src // 2 + t) % outer) * 2 + src % 2) for src in range(n)]
            piece = lax.ppermute(both.astype(jnp.bfloat16), "rep", perm).astype(jnp.float32)
        total = piece if total is None else total + piece
    return total


def gather_blk(panel):
    n = lax.axis_size("blk")
    if n != 4:
        return lax.all_gather(panel, "blk", axis=0, tiled=False), False

    def swap(value, mask):
        return lax.ppermute(value, "blk", [(i, i ^ mask) for i in range(n)])

    across = swap(panel, 2)
    beside = swap(panel, 1)
    diagonal = swap(across, 1)
    return jnp.stack([panel, beside, across, diagonal]), True


def make_body():
    def body(features, weight_one, weight_two, tile_values, tile_rows, tile_cols, tile_count):
        tile_vals = tile_values[0, 0]
        tile_row = tile_rows[0, 0]
        tile_col = tile_cols[0, 0]
        live_count = tile_count[0, 0]
        replicas = lax.axis_size("rep")
        hidden = features
        for layer_id in range(2):
            weight = weight_one if layer_id == 0 else weight_two
            panel = jnp.dot(hidden, weight, preferred_element_type=jnp.float32).astype(jnp.bfloat16)
            blocks, xor_order = gather_blk(panel)
            partial = aggregate(blocks, tile_vals, tile_row, tile_col, live_count, replicas, xor_order)
            summed = exchange_rep(partial)
            if layer_id == 0:
                hidden = jnp.maximum(summed, 0.0).astype(jnp.bfloat16)
            else:
                return summed.astype(jnp.bfloat16)

    return body


def solution(mesh):
    in_specs = (
        P(("blk", "rep"), None),
        P(),
        P(),
        P("blk", "rep", None, None, None),
        P("blk", "rep", None),
        P("blk", "rep", None),
        P("blk", "rep"),
    )
    out_specs = P(("blk", "rep"), None)
    return jax.shard_map(make_body(), mesh=mesh, in_specs=in_specs, out_specs=out_specs, check_vma=False)
```
